256 devices in a mesh: lat: 16 (over y, x_lo, core), lon: 16 (over x_hi, z).
Axes of the slice: x: 4 (x_hi: 2, x_lo: 2; x = x_hi * 2 + x_lo), y: 4, z: 8, core: 2. Of those that a mesh axis runs over, the one named last changes fastest.
Arguments:
- fields: bfloat16 [64, 2048, 192], P('lat', 'lon'), may hold values from -6 to 6
- kernel_first: bfloat16 [9, 192, 192], replicated, may hold values from -0.15625 to 0.15625
- kernel_second: bfloat16 [9, 192, 192], replicated, may hold values from -0.15625 to 0.15625
- kernel_third: bfloat16 [9, 192, 192], replicated, may hold values from -0.15625 to 0.15625
- cotangent: bfloat16 [64, 2048, 192], P('lat', 'lon'), may hold values from -6 to 6
Outputs:
- output: float32 [64, 2048, 192], P('lat', 'lon')
- field_grad: float32 [64, 2048, 192], P('lat', 'lon')
- grad_first: float32 [9, 192, 192], P(None, None, 'lat')
- grad_second: float32 [9, 192, 192], P(None, None, 'lat')
- grad_third: float32 [9, 192, 192], P(None, None, 'lat')
The draws below stay inside these ranges and needn't reach their ends.
All inputs are finite; a program needn't handle non-finite values.
Results may differ from the reference program's by a relative error of at most 0.0049.
Values may be sent and summed in bfloat16 or wider, within the bound.
No kernel may reach another device: no remote copies, remote signals or barrier semaphores. Data moves between devices by JAX's collectives and lax.ppermute only.
A program may use at most 64 MiB of HBM per device.

```python
import jax
import jax.numpy as jnp

C = 192
NLAT = 64
NLON = 2048


def raised(entries, rng, source, target, parts, factor):
    def block_of(dim):
        return (jnp.arange(entries.shape[dim]) // (entries.shape[dim] // parts)).reshape((-1,) + (1,) * (entries.ndim - 1 - dim))

    first = jax.random.permutation(rng, parts)[block_of(target)]
    other_side = (block_of(target) + parts // 2) % parts
    return jnp.where((block_of(source) == first) | (block_of(source) == other_side), factor * entries, entries)


def level_of(key, dims, cuts, least, top_value):
    loudness, own = 1.0, jax.random.fold_in(key, 6)
    for dim, shards_of in cuts:
        draws = jnp.exp(jax.random.uniform(jax.random.fold_in(own, dim), (shards_of,), jnp.float32, least / len(cuts), top_value / len(cuts)))
        loudness = loudness * jnp.repeat(draws, dims[dim] // shards_of).reshape([-1 if axis == dim else 1 for axis in range(len(dims))])
    return loudness


def noise(key, dims, deviation, reach, split=(), dtype=jnp.bfloat16):
    result = jax.random.normal(key, dims, jnp.float32) * deviation
    if len(split) > 0:
        result = level_of(key, dims, split, -0.22, 0.18) * result
    return jnp.clip(result, min=-reach, max=reach).astype(dtype)


def bell_draw_with(stream_key, dims, scale, bound, shards, heavy, dtype=jnp.bfloat16):
    entries = scale * jax.random.normal(stream_key, dims, jnp.float32)
    if shards:
        entries = entries * level_of(stream_key, dims, shards, -0.22, 0.18)
    return jnp.clip(raised(entries, jax.random.fold_in(stream_key, 3), *heavy), -bound, bound).astype(dtype)


def setup_inputs(seed: int = 0) -> dict:
    keys = jax.random.split(jax.random.key(seed), 6)
    fields = noise(keys[0], (NLAT, NLON, C), 1.0, 6.0, ((0, 16), (1, 16)))
    kernel_first = noise(keys[1], (9, C, C), (9 * C) ** -0.5, 0.15625)
    kernel_second = noise(keys[2], (9, C, C), (9 * C) ** -0.5, 0.15625)
    kernel_third = noise(keys[3], (9, C, C), (9 * C) ** -0.5, 0.15625)
    cotangent = bell_draw_with(keys[4], (NLAT, NLON, C), 1.0, 6.0, ((0, 16), (1, 16)), (0, 2, 16, 2.0))
    return dict(fields=fields, kernel_first=kernel_first, kernel_second=kernel_second, kernel_third=kernel_third, cotangent=cotangent)


def gelu(z):
    return 0.5 * z * (1.0 + jax.scipy.special.erf(z * 0.7071067811865476))

def gelu_slope(z):
    return 0.5 * (1.0 + jax.scipy.special.erf(z * 0.7071067811865476)) + z * jnp.exp(-0.5 * z * z) * 0.3989422804014327

def pad_grid(field):
    field = jnp.pad(field, ((1, 1), (0, 0), (0, 0)))
    return jnp.concatenate([field[:, -1:], field, field[:, :1]], axis=1)

def forward_conv(field, kernel):
    padded = pad_grid(field)
    total = jnp.zeros((NLAT * NLON, C), jnp.float32)
    for tap in range(9):
        shift_a, shift_b = divmod(tap, 3)
        piece = padded[shift_a:shift_a + NLAT, shift_b:shift_b + NLON].reshape(NLAT * NLON, C)
        total = total + jnp.dot(piece, kernel[tap], preferred_element_type=jnp.float32)
    return total.reshape(NLAT, NLON, C)

def adjoint_conv(field, kernel):
    padded = pad_grid(field)
    total = jnp.zeros((NLAT * NLON, C), jnp.float32)
    for tap in range(9):
        shift_a, shift_b = divmod(tap, 3)
        piece = padded[2 - shift_a:2 - shift_a + NLAT, 2 - shift_b:2 - shift_b + NLON].reshape(NLAT * NLON, C)
        total = total + jnp.dot(piece, kernel[tap].T, preferred_element_type=jnp.float32)
    return total.reshape(NLAT, NLON, C)

def kernel_grad(field, delta):
    padded = pad_grid(field)
    flat_delta = delta.reshape(NLAT * NLON, C)
    scale = 1.0 / float(NLAT * NLON) ** 0.5
    terms = []
    for tap in range(9):
        shift_a, shift_b = divmod(tap, 3)
        piece = padded[shift_a:shift_a + NLAT, shift_b:shift_b + NLON].reshape(NLAT * NLON, C)
        terms.append(jnp.dot(piece.T, flat_delta, preferred_element_type=jnp.float32) * scale)
    return jnp.stack(terms)

def reference(fields, kernel_first, kernel_second, kernel_third, cotangent):
    pre_first = forward_conv(fields, kernel_first)
    act_first = gelu(pre_first).astype(jnp.bfloat16)
    pre_second = forward_conv(act_first, kernel_second)
    act_second = gelu(pre_second).astype(jnp.bfloat16)
    output = forward_conv(act_second, kernel_third)
    grad_third = kernel_grad(act_second, cotangent)
    delta_second = (adjoint_conv(cotangent, kernel_third) * gelu_slope(pre_second)).astype(jnp.bfloat16)
    grad_second = kernel_grad(act_first, delta_second)
    delta_first = (adjoint_conv(delta_second, kernel_second) * gelu_slope(pre_first)).astype(jnp.bfloat16)
    grad_first = kernel_grad(fields, delta_first)
    field_grad = adjoint_conv(delta_first, kernel_first)
    return (output, field_grad, grad_first, grad_second, grad_third)
```

```python
import jax
import jax.numpy as jnp
from jax import lax
from jax.sharding import PartitionSpec as P


def pad_rim(x):
    nlat, nlon = lax.axis_size("lat"), lax.axis_size("lon")
    both = ("lat", "lon")

    def lin(i, j):
        return i * nlon + j

    def pairs(di, dj):
        out = []
        for i in range(nlat):
            if 0 <= i + di < nlat:
                for j in range(nlon):
                    out.append((lin(i, j), lin(i + di, (j + dj) % nlon)))
        return out

    lon_up = [(j, (j + 1) % nlon) for j in range(nlon)]
    lon_down = [(j, (j - 1) % nlon) for j in range(nlon)]
    lat_up = [(i, i + 1) for i in range(nlat - 1)]
    lat_down = [(i + 1, i) for i in range(nlat - 1)]
    left = lax.ppermute(x[:, -1:], "lon", lon_up)
    right = lax.ppermute(x[:, :1], "lon", lon_down)
    top = lax.ppermute(x[-1:], "lat", lat_up)
    bottom = lax.ppermute(x[:1], "lat", lat_down)
    top_left = lax.ppermute(x[-1:, -1:], both, pairs(1, 1))
    top_right = lax.ppermute(x[-1:, :1], both, pairs(1, -1))
    bottom_left = lax.ppermute(x[:1, -1:], both, pairs(-1, 1))
    bottom_right = lax.ppermute(x[:1, :1], both, pairs(-1, -1))
    upper = jnp.concatenate([top_left, top, top_right], axis=1)
    lower = jnp.concatenate([bottom_left, bottom, bottom_right], axis=1)
    middle = jnp.concatenate([left, x, right], axis=1)
    return jnp.concatenate([upper, middle, lower], axis=0)


def gelu(z):
    return 0.5 * z * (1.0 + jax.scipy.special.erf(z * 0.7071067811865476))


def gelu_slope(z):
    return (
        0.5 * (1.0 + jax.scipy.special.erf(z * 0.7071067811865476))
        + z * jnp.exp(-0.5 * z * z) * 0.3989422804014327
    )


def forward_conv(padded, kernel, out_rows, out_cols):
    total = jnp.zeros((out_rows, out_cols, kernel.shape[2]), jnp.float32)
    for tap in range(9):
        shift_a, shift_b = divmod(tap, 3)
        piece = padded[shift_a : shift_a + out_rows, shift_b : shift_b + out_cols]
        total = total + jnp.einsum(
            "rci,io->rco", piece, kernel[tap], preferred_element_type=jnp.float32
        )
    return total


def adjoint_conv(padded, kernel, out_rows, out_cols):
    total = jnp.zeros((out_rows, out_cols, kernel.shape[1]), jnp.float32)
    for tap in range(9):
        shift_a, shift_b = divmod(tap, 3)
        piece = padded[2 - shift_a : 2 - shift_a + out_rows, 2 - shift_b : 2 - shift_b + out_cols]
        total = total + jnp.einsum(
            "rco,io->rci", piece, kernel[tap], preferred_element_type=jnp.float32
        )
    return total


def halve(x, axis):
    n = lax.axis_size(axis)
    bits = n.bit_length() - 1
    me = lax.axis_index(axis)
    x = x.reshape((2,) * bits + x.shape[1:])
    x = x.transpose(tuple(range(bits - 1, -1, -1)) + tuple(range(bits, x.ndim)))
    for b in range(bits):
        mine = (me >> b) & 1
        keep = lax.dynamic_index_in_dim(x, mine, 0, keepdims=False)
        send = lax.dynamic_index_in_dim(x, 1 - mine, 0, keepdims=False)
        x = keep + lax.ppermute(send, axis, [(i, i ^ (1 << b)) for i in range(n)])
    return x


def all_sum(x, axis):
    n = lax.axis_size(axis)
    for b in range(n.bit_length() - 1):
        x = x + lax.ppermute(x, axis, [(i, i ^ (1 << b)) for i in range(n)])
    return x


def kernel_grad(padded, delta):
    own_rows, own_cols = (delta.shape[0], delta.shape[1])
    cells = own_rows * lax.axis_size("lat") * own_cols * lax.axis_size("lon")
    scale = 1.0 / float(cells) ** 0.5
    terms = []
    for tap in range(9):
        shift_a, shift_b = divmod(tap, 3)
        piece = padded[shift_a : shift_a + own_rows, shift_b : shift_b + own_cols]
        terms.append(
            jnp.einsum("rci,rco->oi", piece, delta, preferred_element_type=jnp.float32) * scale
        )
    local_term = jnp.stack(terms, axis=1)
    n_out, taps, n_in = local_term.shape
    nlat = lax.axis_size("lat")
    owned = halve(local_term.reshape(nlat, (n_out // nlat) * taps * n_in), "lat")
    owned = all_sum(owned, "lon")
    return owned.reshape(n_out // nlat, taps, n_in).transpose(1, 2, 0)


def on_device(fields, kernel_first, kernel_second, kernel_third, cotangent):
    own_rows, own_cols = (fields.shape[0], fields.shape[1])
    fields_pad = pad_rim(fields)
    cotangent_pad = pad_rim(cotangent)
    pre_first = forward_conv(fields_pad, kernel_first, own_rows, own_cols)
    act_first_pad = pad_rim(gelu(pre_first).astype(jnp.bfloat16))
    pre_second = forward_conv(act_first_pad, kernel_second, own_rows, own_cols)
    act_second_pad = pad_rim(gelu(pre_second).astype(jnp.bfloat16))
    delta_second = (
        adjoint_conv(cotangent_pad, kernel_third, own_rows, own_cols) * gelu_slope(pre_second)
    ).astype(jnp.bfloat16)
    delta_second_pad = pad_rim(delta_second)
    output = forward_conv(act_second_pad, kernel_third, own_rows, own_cols)
    grad_third = kernel_grad(act_second_pad, cotangent)
    delta_first = (
        adjoint_conv(delta_second_pad, kernel_second, own_rows, own_cols) * gelu_slope(pre_first)
    ).astype(jnp.bfloat16)
    grad_second = kernel_grad(act_first_pad, delta_second)
    delta_first_pad = pad_rim(delta_first)
    field_grad = adjoint_conv(delta_first_pad, kernel_first, own_rows, own_cols)
    grad_first = kernel_grad(fields_pad, delta_first)
    return (output, field_grad, grad_first, grad_second, grad_third)


def solution(mesh):
    in_specs = (P("lat", "lon", None), P(), P(), P(), P("lat", "lon", None))
    out_specs = (
        P("lat", "lon", None),
        P("lat", "lon", None),
        P(None, None, "lat"),
        P(None, None, "lat"),
        P(None, None, "lat"),
    )
    return jax.shard_map(
        on_device, mesh=mesh, in_specs=in_specs, out_specs=out_specs, check_vma=False
    )
```

```python
import jax
import jax.numpy as jnp
from jax import lax
from jax.sharding import PartitionSpec as P


def exchange(x, h):
    nlat, nlon = lax.axis_size("lat"), lax.axis_size("lon")
    left = lax.ppermute(x[:, -h:], "lon", [(j, (j + 1) % nlon) for j in range(nlon)])
    right = lax.ppermute(x[:, :h], "lon", [(j, (j - 1) % nlon) for j in range(nlon)])
    x = jnp.concatenate([left, x, right], axis=1)
    top = lax.ppermute(x[-h:], "lat", [(i, i + 1) for i in range(nlat - 1)])
    bottom = lax.ppermute(x[:h], "lat", [(i + 1, i) for i in range(nlat - 1)])
    return jnp.concatenate([top, x, bottom], axis=0)


def inside(x, own_rows, h):
    first = lax.axis_index("lat") * own_rows - h
    rows = first + lax.broadcasted_iota(jnp.int32, (x.shape[0], 1, 1), 0)
    keep = (rows >= 0) & (rows < own_rows * lax.axis_size("lat"))
    return jnp.where(keep, x, jnp.zeros_like(x))


def crop(x, h):
    return x[h : x.shape[0] - h, h : x.shape[1] - h]


def gelu(z):
    return 0.5 * z * (1.0 + jax.scipy.special.erf(z * 0.7071067811865476))


def gelu_slope(z):
    return (
        0.5 * (1.0 + jax.scipy.special.erf(z * 0.7071067811865476))
        + z * jnp.exp(-0.5 * z * z) * 0.3989422804014327
    )


def forward_conv(padded, kernel):
    taps, n_in, n_out = kernel.shape
    w = kernel.reshape(3, 3, n_in, n_out)
    return lax.conv_general_dilated(
        padded[None], w, (1, 1), "VALID", dimension_numbers=("NHWC", "HWIO", "NHWC"),
        preferred_element_type=jnp.float32,
    )[0]


def adjoint_conv(padded, kernel):
    taps, n_in, n_out = kernel.shape
    w = kernel.reshape(3, 3, n_in, n_out)[::-1, ::-1].transpose(0, 1, 3, 2)
    return lax.conv_general_dilated(
        padded[None], w, (1, 1), "VALID", dimension_numbers=("NHWC", "HWIO", "NHWC"),
        preferred_element_type=jnp.float32,
    )[0]


def halve(x, axis):
    n = lax.axis_size(axis)
    bits = n.bit_length() - 1
    me = lax.axis_index(axis)
    x = x.reshape((2,) * bits + x.shape[1:])
    x = x.transpose(tuple(range(bits - 1, -1, -1)) + tuple(range(bits, x.ndim)))
    for b in range(bits):
        mine = (me >> b) & 1
        keep = lax.dynamic_index_in_dim(x, mine, 0, keepdims=False)
        send = lax.dynamic_index_in_dim(x, 1 - mine, 0, keepdims=False)
        x = keep + lax.ppermute(send, axis, [(i, i ^ (1 << b)) for i in range(n)])
    return x


def all_sum(x, axis):
    n = lax.axis_size(axis)
    for b in range(n.bit_length() - 1):
        x = x + lax.ppermute(x, axis, [(i, i ^ (1 << b)) for i in range(n)])
    return x


def kernel_grad(padded, delta):
    own_rows, own_cols = (delta.shape[0], delta.shape[1])
    cells = own_rows * lax.axis_size("lat") * own_cols * lax.axis_size("lon")
    scale = 1.0 / float(cells) ** 0.5
    terms = []
    for tap in range(9):
        shift_a, shift_b = divmod(tap, 3)
        piece = padded[shift_a : shift_a + own_rows, shift_b : shift_b + own_cols]
        terms.append(
            jnp.einsum("rci,rco->oi", piece, delta, preferred_element_type=jnp.float32) * scale
        )
    local_term = jnp.stack(terms, axis=1)
    n_out, taps, n_in = local_term.shape
    nlat = lax.axis_size("lat")
    owned = halve(local_term.reshape(nlat, (n_out // nlat) * taps * n_in), "lat")
    owned = all_sum(owned, "lon")
    return owned.reshape(n_out // nlat, taps, n_in).transpose(1, 2, 0)


def on_device(fields, kernel_first, kernel_second, kernel_third, cotangent):
    own_rows = fields.shape[0]
    width = fields.shape[2]
    both = exchange(jnp.concatenate([fields, cotangent], axis=2), 4)
    fields_4, cotangent_3 = both[..., :width], crop(both[..., width:], 1)
    pre_first = forward_conv(fields_4, kernel_first)
    act_first = inside(gelu(pre_first).astype(jnp.bfloat16), own_rows, 3)
    pre_second = forward_conv(act_first, kernel_second)
    act_second = inside(gelu(crop(pre_second, 1)).astype(jnp.bfloat16), own_rows, 1)
    output = forward_conv(act_second, kernel_third)
    grad_third = kernel_grad(act_second, crop(cotangent_3, 3))
    delta_second = inside(
        (adjoint_conv(cotangent_3, kernel_third) * gelu_slope(pre_second)).astype(jnp.bfloat16),
        own_rows, 2,
    )
    delta_first = inside(
        (adjoint_conv(delta_second, kernel_second) * gelu_slope(crop(pre_first, 2))).astype(
            jnp.bfloat16
        ),
        own_rows, 1,
    )
    grad_second = kernel_grad(crop(act_first, 2), crop(delta_second, 2))
    field_grad = adjoint_conv(delta_first, kernel_first)
    grad_first = kernel_grad(crop(fields_4, 3), crop(delta_first, 1))
    return (output, field_grad, grad_first, grad_second, grad_third)


def solution(mesh):
    in_specs = (P("lat", "lon", None), P(), P(), P(), P("lat", "lon", None))
    out_specs = (
        P("lat", "lon", None),
        P("lat", "lon", None),
        P(None, None, "lat"),
        P(None, None, "lat"),
        P(None, None, "lat"),
    )
    return jax.shard_map(
        on_device, mesh=mesh, in_specs=in_specs, out_specs=out_specs, check_vma=False
    )
```

```python
import jax
import jax.numpy as jnp
from jax import lax
from jax.sharding import PartitionSpec as P


def exchange(x, h):
    nlat, nlon = lax.axis_size("lat"), lax.axis_size("lon")
    left = lax.ppermute(x[:, -h:], "lon", [(j, (j + 1) % nlon) for j in range(nlon)])
    right = lax.ppermute(x[:, :h], "lon", [(j, (j - 1) % nlon) for j in range(nlon)])
    x = jnp.concatenate([left, x, right], axis=1)
    top = lax.ppermute(x[-h:], "lat", [(i, i + 1) for i in range(nlat - 1)])
    bottom = lax.ppermute(x[:h], "lat", [(i + 1, i) for i in range(nlat - 1)])
    return jnp.concatenate([top, x, bottom], axis=0)


def inside(x, own_rows, h):
    first = lax.axis_index("lat") * own_rows - h
    rows = first + lax.broadcasted_iota(jnp.int32, (x.shape[0], 1, 1), 0)
    keep = (rows >= 0) & (rows < own_rows * lax.axis_size("lat"))
    return jnp.where(keep, x, jnp.zeros_like(x))


def crop(x, h):
    return x[h : x.shape[0] - h, h : x.shape[1] - h]


def gelu(z):
    return 0.5 * z * (1.0 + jax.scipy.special.erf(z * 0.7071067811865476))


def gelu_slope(z):
    return (
        0.5 * (1.0 + jax.scipy.special.erf(z * 0.7071067811865476))
        + z * jnp.exp(-0.5 * z * z) * 0.3989422804014327
    )


def forward_conv(padded, kernel):
    out_rows, out_cols = (padded.shape[0] - 2, padded.shape[1] - 2)
    total = jnp.zeros((out_rows, out_cols, kernel.shape[2]), jnp.float32)
    for tap in range(9):
        shift_a, shift_b = divmod(tap, 3)
        piece = padded[shift_a : shift_a + out_rows, shift_b : shift_b + out_cols]
        total = total + jnp.einsum(
            "rci,io->rco", piece, kernel[tap], preferred_element_type=jnp.float32
        )
    return total


def adjoint_conv(padded, kernel):
    out_rows, out_cols = (padded.shape[0] - 2, padded.shape[1] - 2)
    total = jnp.zeros((out_rows, out_cols, kernel.shape[1]), jnp.float32)
    for tap in range(9):
        shift_a, shift_b = divmod(tap, 3)
        piece = padded[2 - shift_a : 2 - shift_a + out_rows, 2 - shift_b : 2 - shift_b + out_cols]
        total = total + jnp.einsum(
            "rco,io->rci", piece, kernel[tap], preferred_element_type=jnp.float32
        )
    return total


def halve(x, axis):
    n = lax.axis_size(axis)
    bits = n.bit_length() - 1
    me = lax.axis_index(axis)
    x = x.reshape((2,) * bits + x.shape[1:])
    x = x.transpose(tuple(range(bits - 1, -1, -1)) + tuple(range(bits, x.ndim)))
    for b in range(bits):
        mine = (me >> b) & 1
        keep = lax.dynamic_index_in_dim(x, mine, 0, keepdims=False)
        send = lax.dynamic_index_in_dim(x, 1 - mine, 0, keepdims=False)
        x = keep + lax.ppermute(send, axis, [(i, i ^ (1 << b)) for i in range(n)])
    return x


def all_sum(x, axis):
    n = lax.axis_size(axis)
    for b in range(n.bit_length() - 1):
        x = x + lax.ppermute(x, axis, [(i, i ^ (1 << b)) for i in range(n)])
    return x


def kernel_grad(padded, delta):
    own_rows, own_cols = (delta.shape[0], delta.shape[1])
    cells = own_rows * lax.axis_size("lat") * own_cols * lax.axis_size("lon")
    scale = 1.0 / float(cells) ** 0.5
    terms = []
    for tap in range(9):
        shift_a, shift_b = divmod(tap, 3)
        piece = padded[shift_a : shift_a + own_rows, shift_b : shift_b + own_cols]
        terms.append(
            jnp.einsum("rci,rco->oi", piece, delta, preferred_element_type=jnp.float32) * scale
        )
    local_term = jnp.stack(terms, axis=1)
    n_out, taps, n_in = local_term.shape
    nlat = lax.axis_size("lat")
    owned = halve(local_term.reshape(nlat, -1, 128), "lat")
    owned = all_sum(owned, "lon")
    return owned.reshape(n_out // nlat, taps, n_in).transpose(1, 2, 0)


def on_device(fields, kernel_first, kernel_second, kernel_third, cotangent):
    own_rows = fields.shape[0]
    width = fields.shape[2]
    both = exchange(jnp.concatenate([fields, cotangent], axis=2), 4)
    fields_4, cotangent_3 = both[..., :width], crop(both[..., width:], 1)
    pre_first = forward_conv(fields_4, kernel_first)
    act_first = inside(gelu(pre_first).astype(jnp.bfloat16), own_rows, 3)
    pre_second = forward_conv(act_first, kernel_second)
    act_second = inside(gelu(crop(pre_second, 1)).astype(jnp.bfloat16), own_rows, 1)
    output = forward_conv(act_second, kernel_third)
    grad_third = kernel_grad(act_second, crop(cotangent_3, 3))
    delta_second = inside(
        (adjoint_conv(cotangent_3, kernel_third) * gelu_slope(pre_second)).astype(jnp.bfloat16),
        own_rows, 2,
    )
    delta_first = inside(
        (adjoint_conv(delta_second, kernel_second) * gelu_slope(crop(pre_first, 2))).astype(
            jnp.bfloat16
        ),
        own_rows, 1,
    )
    grad_second = kernel_grad(crop(act_first, 2), crop(delta_second, 2))
    field_grad = adjoint_conv(delta_first, kernel_first)
    grad_first = kernel_grad(crop(fields_4, 3), crop(delta_first, 1))
    return (output, field_grad, grad_first, grad_second, grad_third)


def solution(mesh):
    in_specs = (P("lat", "lon", None), P(), P(), P(), P("lat", "lon", None))
    out_specs = (
        P("lat", "lon", None),
        P("lat", "lon", None),
        P(None, None, "lat"),
        P(None, None, "lat"),
        P(None, None, "lat"),
    )
    return jax.shard_map(
        on_device, mesh=mesh, in_specs=in_specs, out_specs=out_specs, check_vma=False
    )
```

```python
import jax
import jax.numpy as jnp
from jax import lax
from jax.sharding import PartitionSpec as P


def exchange(x, h):
    nlat, nlon = lax.axis_size("lat"), lax.axis_size("lon")
    left = lax.ppermute(x[:, -h:], "lon", [(j, (j + 1) % nlon) for j in range(nlon)])
    right = lax.ppermute(x[:, :h], "lon", [(j, (j - 1) % nlon) for j in range(nlon)])
    x = jnp.concatenate([left, x, right], axis=1)
    top = lax.ppermute(x[-h:], "lat", [(i, i + 1) for i in range(nlat - 1)])
    bottom = lax.ppermute(x[:h], "lat", [(i + 1, i) for i in range(nlat - 1)])
    return jnp.concatenate([top, x, bottom], axis=0)


def inside(x, own_rows, h):
    first = lax.axis_index("lat") * own_rows - h
    rows = first + lax.broadcasted_iota(jnp.int32, (x.shape[0], 1, 1), 0)
    keep = (rows >= 0) & (rows < own_rows * lax.axis_size("lat"))
    return jnp.where(keep, x, jnp.zeros_like(x))


def crop(x, h):
    return x[h : x.shape[0] - h, h : x.shape[1] - h]


def gelu(z):
    return 0.5 * z * (1.0 + jax.scipy.special.erf(z * 0.7071067811865476))


def gelu_slope(z):
    return (
        0.5 * (1.0 + jax.scipy.special.erf(z * 0.7071067811865476))
        + z * jnp.exp(-0.5 * z * z) * 0.3989422804014327
    )


def forward_conv(padded, kernel):
    out_rows, out_cols = (padded.shape[0] - 2, padded.shape[1] - 2)
    total = jnp.zeros((out_rows, out_cols, kernel.shape[2]), jnp.float32)
    for tap in range(9):
        shift_a, shift_b = divmod(tap, 3)
        piece = padded[shift_a : shift_a + out_rows, shift_b : shift_b + out_cols]
        total = total + jnp.einsum(
            "rci,io->rco", piece, kernel[tap], preferred_element_type=jnp.float32
        )
    return total


def adjoint_conv(padded, kernel):
    out_rows, out_cols = (padded.shape[0] - 2, padded.shape[1] - 2)
    total = jnp.zeros((out_rows, out_cols, kernel.shape[1]), jnp.float32)
    for tap in range(9):
        shift_a, shift_b = divmod(tap, 3)
        piece = padded[2 - shift_a : 2 - shift_a + out_rows, 2 - shift_b : 2 - shift_b + out_cols]
        total = total + jnp.einsum(
            "rco,io->rci", piece, kernel[tap], preferred_element_type=jnp.float32
        )
    return total


def gray(n_bits, low):
    def label(i):
        ring = (i >> low) & ((1 << n_bits) - 1)
        return (i & ~(((1 << n_bits) - 1) << low)) | ((ring ^ (ring >> 1)) << low)
    return label


def labels(axis):
    n = lax.axis_size(axis)
    label = gray(2, 2) if axis == "lat" else gray(3, 0)
    lab = [label(i) for i in range(n)]
    pos = [0] * n
    for i, l in enumerate(lab):
        pos[l] = i
    return lab, pos


def halve(x, axis):
    n = lax.axis_size(axis)
    bits = n.bit_length() - 1
    lab, pos = labels(axis)
    x = jnp.stack([x[pos[l]] for l in range(n)])
    me = jnp.asarray(lab, jnp.int32)[lax.axis_index(axis)]
    x = x.reshape((2,) * bits + x.shape[1:])
    x = x.transpose(tuple(range(bits - 1, -1, -1)) + tuple(range(bits, x.ndim)))
    for b in range(bits):
        mine = (me >> b) & 1
        keep = lax.dynamic_index_in_dim(x, mine, 0, keepdims=False)
        send = lax.dynamic_index_in_dim(x, 1 - mine, 0, keepdims=False)
        x = keep + lax.ppermute(send, axis, [(i, pos[lab[i] ^ (1 << b)]) for i in range(n)])
    return x


def all_sum(x, axis):
    n = lax.axis_size(axis)
    lab, pos = labels(axis)
    for b in range(n.bit_length() - 1):
        x = x + lax.ppermute(x, axis, [(i, pos[lab[i] ^ (1 << b)]) for i in range(n)])
    return x


def kernel_grad(padded, delta):
    own_rows, own_cols = (delta.shape[0], delta.shape[1])
    cells = own_rows * lax.axis_size("lat") * own_cols * lax.axis_size("lon")
    scale = 1.0 / float(cells) ** 0.5
    terms = []
    for tap in range(9):
        shift_a, shift_b = divmod(tap, 3)
        piece = padded[shift_a : shift_a + own_rows, shift_b : shift_b + own_cols]
        terms.append(
            jnp.einsum("rci,rco->oi", piece, delta, preferred_element_type=jnp.float32) * scale
        )
    local_term = jnp.stack(terms, axis=1)
    n_out, taps, n_in = local_term.shape
    nlat = lax.axis_size("lat")
    owned = halve(local_term.reshape(nlat, -1, 128), "lat")
    owned = all_sum(owned, "lon")
    return owned.reshape(n_out // nlat, taps, n_in).transpose(1, 2, 0)


def on_device(fields, kernel_first, kernel_second, kernel_third, cotangent):
    own_rows = fields.shape[0]
    width = fields.shape[2]
    both = exchange(jnp.concatenate([fields, cotangent], axis=2), 4)
    fields_4, cotangent_3 = both[..., :width], crop(both[..., width:], 1)
    pre_first = forward_conv(fields_4, kernel_first)
    act_first = inside(gelu(pre_first).astype(jnp.bfloat16), own_rows, 3)
    pre_second = forward_conv(act_first, kernel_second)
    act_second = inside(gelu(crop(pre_second, 1)).astype(jnp.bfloat16), own_rows, 1)
    output = forward_conv(act_second, kernel_third)
    grad_third = kernel_grad(act_second, crop(cotangent_3, 3))
    delta_second = inside(
        (adjoint_conv(cotangent_3, kernel_third) * gelu_slope(pre_second)).astype(jnp.bfloat16),
        own_rows, 2,
    )
    delta_first = inside(
        (adjoint_conv(delta_second, kernel_second) * gelu_slope(crop(pre_first, 2))).astype(
            jnp.bfloat16
        ),
        own_rows, 1,
    )
    grad_second = kernel_grad(crop(act_first, 2), crop(delta_second, 2))
    field_grad = adjoint_conv(delta_first, kernel_first)
    grad_first = kernel_grad(crop(fields_4, 3), crop(delta_first, 1))
    return (output, field_grad, grad_first, grad_second, grad_third)


def solution(mesh):
    in_specs = (P("lat", "lon", None), P(), P(), P(), P("lat", "lon", None))
    out_specs = (
        P("lat", "lon", None),
        P("lat", "lon", None),
        P(None, None, "lat"),
        P(None, None, "lat"),
        P(None, None, "lat"),
    )
    return jax.shard_map(
        on_device, mesh=mesh, in_specs=in_specs, out_specs=out_specs, check_vma=False
    )
```

```python
import jax
import jax.numpy as jnp
from jax import lax
from jax.sharding import PartitionSpec as P


def exchange(x, h):
    nlat, nlon = lax.axis_size("lat"), lax.axis_size("lon")
    left = lax.ppermute(x[:, -h:], "lon", [(j, (j + 1) % nlon) for j in range(nlon)])
    right = lax.ppermute(x[:, :h], "lon", [(j, (j - 1) % nlon) for j in range(nlon)])
    x = jnp.concatenate([left, x, right], axis=1)
    top = lax.ppermute(x[-h:], "lat", [(i, i + 1) for i in range(nlat - 1)])
    bottom = lax.ppermute(x[:h], "lat", [(i + 1, i) for i in range(nlat - 1)])
    return jnp.concatenate([top, x, bottom], axis=0)


def inside(x, own_rows, h):
    first = lax.axis_index("lat") * own_rows - h
    rows = first + lax.broadcasted_iota(jnp.int32, (x.shape[0], 1, 1), 0)
    keep = (rows >= 0) & (rows < own_rows * lax.axis_size("lat"))
    return jnp.where(keep, x, jnp.zeros_like(x))


def crop(x, h):
    return x[h : x.shape[0] - h, h : x.shape[1] - h]


def gelu(z):
    return 0.5 * z * (1.0 + jax.scipy.special.erf(z * 0.7071067811865476))


def gelu_slope(z):
    return (
        0.5 * (1.0 + jax.scipy.special.erf(z * 0.7071067811865476))
        + z * jnp.exp(-0.5 * z * z) * 0.3989422804014327
    )


def forward_conv(padded, kernel):
    out_rows, out_cols = (padded.shape[0] - 2, padded.shape[1] - 2)
    total = jnp.zeros((out_rows, out_cols, kernel.shape[2]), jnp.float32)
    for tap in range(9):
        shift_a, shift_b = divmod(tap, 3)
        piece = padded[shift_a : shift_a + out_rows, shift_b : shift_b + out_cols]
        total = total + jnp.einsum(
            "rci,io->rco", piece, kernel[tap], preferred_element_type=jnp.float32
        )
    return total


def adjoint_conv(padded, kernel):
    out_rows, out_cols = (padded.shape[0] - 2, padded.shape[1] - 2)
    total = jnp.zeros((out_rows, out_cols, kernel.shape[1]), jnp.float32)
    for tap in range(9):
        shift_a, shift_b = divmod(tap, 3)
        piece = padded[2 - shift_a : 2 - shift_a + out_rows, 2 - shift_b : 2 - shift_b + out_cols]
        total = total + jnp.einsum(
            "rco,io->rci", piece, kernel[tap], preferred_element_type=jnp.float32
        )
    return total


def gray(n_bits, low):
    def label(i):
        ring = (i >> low) & ((1 << n_bits) - 1)
        return (i & ~(((1 << n_bits) - 1) << low)) | ((ring ^ (ring >> 1)) << low)
    return label


def labels(axis):
    n = lax.axis_size(axis)
    label = gray(2, 2) if axis == "lat" else gray(3, 0)
    lab = [label(i) for i in range(n)]
    pos = [0] * n
    for i, l in enumerate(lab):
        pos[l] = i
    return lab, pos


def halve(x, axis):
    n = lax.axis_size(axis)
    bits = n.bit_length() - 1
    lab, pos = labels(axis)
    runs, first = [], 0
    for l in range(1, n + 1):
        if l == n or pos[l] != pos[l - 1] + 1:
            runs.append(x[pos[first] : pos[l - 1] + 1])
            first = l
    x = jnp.concatenate(runs) if len(runs) > 1 else x
    me = jnp.asarray(lab, jnp.int32)[lax.axis_index(axis)]
    x = x.reshape((2,) * bits + x.shape[1:])
    x = x.transpose(tuple(range(bits - 1, -1, -1)) + tuple(range(bits, x.ndim)))
    for b in range(bits):
        mine = (me >> b) & 1
        keep = lax.dynamic_index_in_dim(x, mine, 0, keepdims=False)
        send = lax.dynamic_index_in_dim(x, 1 - mine, 0, keepdims=False)
        x = keep + lax.ppermute(send, axis, [(i, pos[lab[i] ^ (1 << b)]) for i in range(n)])
    return x


def all_sum(x, axis):
    n = lax.axis_size(axis)
    lab, pos = labels(axis)
    for b in range(n.bit_length() - 1):
        x = x + lax.ppermute(x, axis, [(i, pos[lab[i] ^ (1 << b)]) for i in range(n)])
    return x


def kernel_grad(padded, delta):
    own_rows, own_cols = (delta.shape[0], delta.shape[1])
    cells = own_rows * lax.axis_size("lat") * own_cols * lax.axis_size("lon")
    scale = 1.0 / float(cells) ** 0.5
    terms = []
    for tap in range(9):
        shift_a, shift_b = divmod(tap, 3)
        piece = padded[shift_a : shift_a + own_rows, shift_b : shift_b + own_cols]
        terms.append(
            jnp.einsum("rci,rco->oi", piece, delta, preferred_element_type=jnp.float32) * scale
        )
    local_term = jnp.stack(terms, axis=1)
    n_out, taps, n_in = local_term.shape
    nlat = lax.axis_size("lat")
    owned = halve(local_term.reshape(nlat, -1, 128), "lat")
    owned = all_sum(owned, "lon")
    return owned.reshape(n_out // nlat, taps, n_in).transpose(1, 2, 0)


def on_device(fields, kernel_first, kernel_second, kernel_third, cotangent):
    own_rows = fields.shape[0]
    width = fields.shape[2]
    both = exchange(jnp.concatenate([fields, cotangent], axis=2), 4)
    fields_4, cotangent_3 = both[..., :width], crop(both[..., width:], 1)
    pre_first = forward_conv(fields_4, kernel_first)
    act_first = inside(gelu(pre_first).astype(jnp.bfloat16), own_rows, 3)
    pre_second = forward_conv(act_first, kernel_second)
    act_second = inside(gelu(crop(pre_second, 1)).astype(jnp.bfloat16), own_rows, 1)
    output = forward_conv(act_second, kernel_third)
    grad_third = kernel_grad(act_second, crop(cotangent_3, 3))
    delta_second = inside(
        (adjoint_conv(cotangent_3, kernel_third) * gelu_slope(pre_second)).astype(jnp.bfloat16),
        own_rows, 2,
    )
    delta_first = inside(
        (adjoint_conv(delta_second, kernel_second) * gelu_slope(crop(pre_first, 2))).astype(
            jnp.bfloat16
        ),
        own_rows, 1,
    )
    grad_second = kernel_grad(crop(act_first, 2), crop(delta_second, 2))
    field_grad = adjoint_conv(delta_first, kernel_first)
    grad_first = kernel_grad(crop(fields_4, 3), crop(delta_first, 1))
    return (output, field_grad, grad_first, grad_second, grad_third)


def solution(mesh):
    in_specs = (P("lat", "lon", None), P(), P(), P(), P("lat", "lon", None))
    out_specs = (
        P("lat", "lon", None),
        P("lat", "lon", None),
        P(None, None, "lat"),
        P(None, None, "lat"),
        P(None, None, "lat"),
    )
    return jax.shard_map(
        on_device, mesh=mesh, in_specs=in_specs, out_specs=out_specs, check_vma=False
    )
```

```python
import jax
import jax.numpy as jnp
from jax import lax
from jax.sharding import PartitionSpec as P


def exchange(x, h):
    nlat, nlon = lax.axis_size("lat"), lax.axis_size("lon")
    left = lax.ppermute(x[:, -h:], "lon", [(j, (j + 1) % nlon) for j in range(nlon)])
    right = lax.ppermute(x[:, :h], "lon", [(j, (j - 1) % nlon) for j in range(nlon)])
    x = jnp.concatenate([left, x, right], axis=1)
    top = lax.ppermute(x[-h:], "lat", [(i, i + 1) for i in range(nlat - 1)])
    bottom = lax.ppermute(x[:h], "lat", [(i + 1, i) for i in range(nlat - 1)])
    return jnp.concatenate([top, x, bottom], axis=0)


def inside(x, own_rows, h):
    first = lax.axis_index("lat") * own_rows - h
    rows = first + lax.broadcasted_iota(jnp.int32, (x.shape[0], 1, 1), 0)
    keep = (rows >= 0) & (rows < own_rows * lax.axis_size("lat"))
    return jnp.where(keep, x, jnp.zeros_like(x))


def crop(x, h):
    return x[h : x.shape[0] - h, h : x.shape[1] - h]


def gelu(z):
    return 0.5 * z * (1.0 + jax.scipy.special.erf(z * 0.7071067811865476))


def gelu_slope(z):
    return (
        0.5 * (1.0 + jax.scipy.special.erf(z * 0.7071067811865476))
        + z * jnp.exp(-0.5 * z * z) * 0.3989422804014327
    )


def forward_conv(padded, kernel):
    out_rows, out_cols = (padded.shape[0] - 2, padded.shape[1] - 2)
    total = jnp.zeros((out_rows, out_cols, kernel.shape[2]), jnp.float32)
    for tap in range(9):
        shift_a, shift_b = divmod(tap, 3)
        piece = padded[shift_a : shift_a + out_rows, shift_b : shift_b + out_cols]
        total = total + jnp.einsum(
            "rci,io->rco", piece, kernel[tap], preferred_element_type=jnp.float32
        )
    return total


def adjoint_conv(padded, kernel):
    out_rows, out_cols = (padded.shape[0] - 2, padded.shape[1] - 2)
    total = jnp.zeros((out_rows, out_cols, kernel.shape[1]), jnp.float32)
    for tap in range(9):
        shift_a, shift_b = divmod(tap, 3)
        piece = padded[2 - shift_a : 2 - shift_a + out_rows, 2 - shift_b : 2 - shift_b + out_cols]
        total = total + jnp.einsum(
            "rco,io->rci", piece, kernel[tap], preferred_element_type=jnp.float32
        )
    return total


def gray(n_bits, low):
    def label(i):
        ring = (i >> low) & ((1 << n_bits) - 1)
        return (i & ~(((1 << n_bits) - 1) << low)) | ((ring ^ (ring >> 1)) << low)
    return label


def labels(axis):
    n = lax.axis_size(axis)
    label = gray(2, 2) if axis == "lat" else gray(3, 0)
    lab = [label(i) for i in range(n)]
    pos = [0] * n
    for i, l in enumerate(lab):
        pos[l] = i
    return lab, pos


def halve(x, axis):
    n = lax.axis_size(axis)
    bits = n.bit_length() - 1
    lab, pos = labels(axis)
    runs, first = [], 0
    for l in range(1, n + 1):
        if l == n or pos[l] != pos[l - 1] + 1:
            runs.append(x[pos[first] : pos[l - 1] + 1])
            first = l
    x = jnp.concatenate(runs) if len(runs) > 1 else x
    me = jnp.asarray(lab, jnp.int32)[lax.axis_index(axis)]
    x = x.reshape((2,) * bits + x.shape[1:])
    x = x.transpose(tuple(range(bits - 1, -1, -1)) + tuple(range(bits, x.ndim)))
    for b in range(bits):
        mine = (me >> b) & 1
        keep = lax.dynamic_index_in_dim(x, mine, 0, keepdims=False)
        send = lax.dynamic_index_in_dim(x, 1 - mine, 0, keepdims=False)
        x = keep + lax.ppermute(send, axis, [(i, pos[lab[i] ^ (1 << b)]) for i in range(n)])
    return x


def all_sum(x, axis):
    n = lax.axis_size(axis)
    lab, pos = labels(axis)
    for b in range(n.bit_length() - 1):
        x = x + lax.ppermute(x, axis, [(i, pos[lab[i] ^ (1 << b)]) for i in range(n)])
    return x


def kernel_grad(padded, delta):
    own_rows, own_cols = (delta.shape[0], delta.shape[1])
    cells = own_rows * lax.axis_size("lat") * own_cols * lax.axis_size("lon")
    scale = 1.0 / float(cells) ** 0.5
    patches = jnp.concatenate(
        [
            padded[shift_a : shift_a + own_rows, shift_b : shift_b + own_cols]
            for shift_a, shift_b in (divmod(tap, 3) for tap in range(9))
        ],
        axis=2,
    )
    local_term = jnp.einsum(
        "rco,rck->ok", delta, patches, preferred_element_type=jnp.float32
    ) * scale
    local_term = local_term.reshape(delta.shape[2], 9, padded.shape[2])
    n_out, taps, n_in = local_term.shape
    nlat = lax.axis_size("lat")
    owned = halve(local_term.reshape(nlat, -1, 128), "lat")
    owned = all_sum(owned, "lon")
    return owned.reshape(n_out // nlat, taps, n_in).transpose(1, 2, 0)


def on_device(fields, kernel_first, kernel_second, kernel_third, cotangent):
    own_rows = fields.shape[0]
    width = fields.shape[2]
    both = exchange(jnp.concatenate([fields, cotangent], axis=2), 4)
    fields_4, cotangent_3 = both[..., :width], crop(both[..., width:], 1)
    pre_first = forward_conv(fields_4, kernel_first)
    act_first = inside(gelu(pre_first).astype(jnp.bfloat16), own_rows, 3)
    pre_second = forward_conv(act_first, kernel_second)
    act_second = inside(gelu(crop(pre_second, 1)).astype(jnp.bfloat16), own_rows, 1)
    output = forward_conv(act_second, kernel_third)
    grad_third = kernel_grad(act_second, crop(cotangent_3, 3))
    delta_second = inside(
        (adjoint_conv(cotangent_3, kernel_third) * gelu_slope(pre_second)).astype(jnp.bfloat16),
        own_rows, 2,
    )
    delta_first = inside(
        (adjoint_conv(delta_second, kernel_second) * gelu_slope(crop(pre_first, 2))).astype(
            jnp.bfloat16
        ),
        own_rows, 1,
    )
    grad_second = kernel_grad(crop(act_first, 2), crop(delta_second, 2))
    field_grad = adjoint_conv(delta_first, kernel_first)
    grad_first = kernel_grad(crop(fields_4, 3), crop(delta_first, 1))
    return (output, field_grad, grad_first, grad_second, grad_third)


def solution(mesh):
    in_specs = (P("lat", "lon", None), P(), P(), P(), P("lat", "lon", None))
    out_specs = (
        P("lat", "lon", None),
        P("lat", "lon", None),
        P(None, None, "lat"),
        P(None, None, "lat"),
        P(None, None, "lat"),
    )
    return jax.shard_map(
        on_device, mesh=mesh, in_specs=in_specs, out_specs=out_specs, check_vma=False
    )
```

```python
import jax
import jax.numpy as jnp
from jax import lax
from jax.sharding import PartitionSpec as P


def exchange(x, h):
    nlat, nlon = lax.axis_size("lat"), lax.axis_size("lon")
    left = lax.ppermute(x[:, -h:], "lon", [(j, (j + 1) % nlon) for j in range(nlon)])
    right = lax.ppermute(x[:, :h], "lon", [(j, (j - 1) % nlon) for j in range(nlon)])
    x = jnp.concatenate([left, x, right], axis=1)
    top = lax.ppermute(x[-h:], "lat", [(i, i + 1) for i in range(nlat - 1)])
    bottom = lax.ppermute(x[:h], "lat", [(i + 1, i) for i in range(nlat - 1)])
    return jnp.concatenate([top, x, bottom], axis=0)


def inside(x, own_rows, h):
    first = lax.axis_index("lat") * own_rows - h
    rows = first + lax.broadcasted_iota(jnp.int32, (x.shape[0], 1, 1), 0)
    keep = (rows >= 0) & (rows < own_rows * lax.axis_size("lat"))
    return jnp.where(keep, x, jnp.zeros_like(x))


def crop(x, h):
    return x[h : x.shape[0] - h, h : x.shape[1] - h]


def gelu(z):
    return 0.5 * z * (1.0 + jax.scipy.special.erf(z * 0.7071067811865476))


def gelu_slope(z):
    return (
        0.5 * (1.0 + jax.scipy.special.erf(z * 0.7071067811865476))
        + z * jnp.exp(-0.5 * z * z) * 0.3989422804014327
    )


def forward_conv(padded, kernel):
    out_rows, out_cols = (padded.shape[0] - 2, padded.shape[1] - 2)
    total = jnp.zeros((out_rows, out_cols, kernel.shape[2]), jnp.float32)
    for tap in range(9):
        shift_a, shift_b = divmod(tap, 3)
        piece = padded[shift_a : shift_a + out_rows, shift_b : shift_b + out_cols]
        total = total + jnp.einsum(
            "rci,io->rco", piece, kernel[tap], preferred_element_type=jnp.float32
        )
    return total


def adjoint_conv(padded, kernel):
    out_rows, out_cols = (padded.shape[0] - 2, padded.shape[1] - 2)
    total = jnp.zeros((out_rows, out_cols, kernel.shape[1]), jnp.float32)
    for tap in range(9):
        shift_a, shift_b = divmod(tap, 3)
        piece = padded[2 - shift_a : 2 - shift_a + out_rows, 2 - shift_b : 2 - shift_b + out_cols]
        total = total + jnp.einsum(
            "rco,io->rci", piece, kernel[tap], preferred_element_type=jnp.float32
        )
    return total


def gray(n_bits, low):
    def label(i):
        ring = (i >> low) & ((1 << n_bits) - 1)
        return (i & ~(((1 << n_bits) - 1) << low)) | ((ring ^ (ring >> 1)) << low)
    return label


def labels(axis):
    n = lax.axis_size(axis)
    label = gray(2, 2) if axis == "lat" else gray(3, 0)
    lab = [label(i) for i in range(n)]
    pos = [0] * n
    for i, l in enumerate(lab):
        pos[l] = i
    return lab, pos


def halve(x, axis, order=None):
    n = lax.axis_size(axis)
    bits = n.bit_length() - 1
    order = tuple(range(bits)) if order is None else tuple(b for b in order if b < bits)
    lab, pos = labels(axis)
    runs, first = [], 0
    for l in range(1, n + 1):
        if l == n or pos[l] != pos[l - 1] + 1:
            runs.append(x[pos[first] : pos[l - 1] + 1])
            first = l
    x = jnp.concatenate(runs) if len(runs) > 1 else x
    me = jnp.asarray(lab, jnp.int32)[lax.axis_index(axis)]
    x = x.reshape((2,) * bits + x.shape[1:])
    x = x.transpose(tuple(bits - 1 - b for b in order) + tuple(range(bits, x.ndim)))
    for b in order:
        mine = (me >> b) & 1
        keep = lax.dynamic_index_in_dim(x, mine, 0, keepdims=False)
        send = lax.dynamic_index_in_dim(x, 1 - mine, 0, keepdims=False)
        x = keep + lax.ppermute(send, axis, [(i, pos[lab[i] ^ (1 << b)]) for i in range(n)])
    return x


def all_sum(x, axis, order=None):
    n = lax.axis_size(axis)
    lab, pos = labels(axis)
    bits = n.bit_length() - 1
    order = tuple(range(bits)) if order is None else tuple(b for b in order if b < bits)
    for b in order:
        x = x + lax.ppermute(x, axis, [(i, pos[lab[i] ^ (1 << b)]) for i in range(n)])
    return x


def kernel_grad(padded, delta, lat_order, lon_order):
    own_rows, own_cols = (delta.shape[0], delta.shape[1])
    cells = own_rows * lax.axis_size("lat") * own_cols * lax.axis_size("lon")
    scale = 1.0 / float(cells) ** 0.5
    terms = []
    for tap in range(9):
        shift_a, shift_b = divmod(tap, 3)
        piece = padded[shift_a : shift_a + own_rows, shift_b : shift_b + own_cols]
        terms.append(
            jnp.einsum("rci,rco->oi", piece, delta, preferred_element_type=jnp.float32) * scale
        )
    local_term = jnp.stack(terms, axis=1)
    n_out, taps, n_in = local_term.shape
    nlat = lax.axis_size("lat")
    owned = halve(local_term.reshape(nlat, -1, 128), "lat", lat_order)
    owned = all_sum(owned, "lon", lon_order)
    return owned.reshape(n_out // nlat, taps, n_in).transpose(1, 2, 0)


def on_device(fields, kernel_first, kernel_second, kernel_third, cotangent):
    own_rows = fields.shape[0]
    width = fields.shape[2]
    both = exchange(jnp.concatenate([fields, cotangent], axis=2), 4)
    fields_4, cotangent_3 = both[..., :width], crop(both[..., width:], 1)
    pre_first = forward_conv(fields_4, kernel_first)
    act_first = inside(gelu(pre_first).astype(jnp.bfloat16), own_rows, 3)
    pre_second = forward_conv(act_first, kernel_second)
    act_second = inside(gelu(crop(pre_second, 1)).astype(jnp.bfloat16), own_rows, 1)
    output = forward_conv(act_second, kernel_third)
    grad_third = kernel_grad(act_second, crop(cotangent_3, 3), (0, 1, 2, 3), (0, 1, 2, 3))
    delta_second = inside(
        (adjoint_conv(cotangent_3, kernel_third) * gelu_slope(pre_second)).astype(jnp.bfloat16),
        own_rows, 2,
    )
    delta_first = inside(
        (adjoint_conv(delta_second, kernel_second) * gelu_slope(crop(pre_first, 2))).astype(
            jnp.bfloat16
        ),
        own_rows, 1,
    )
    grad_second = kernel_grad(crop(act_first, 2), crop(delta_second, 2), (0, 2, 1, 3), (1, 2, 3, 0))
    field_grad = adjoint_conv(delta_first, kernel_first)
    grad_first = kernel_grad(crop(fields_4, 3), crop(delta_first, 1), (0, 3, 2, 1), (2, 3, 0, 1))
    return (output, field_grad, grad_first, grad_second, grad_third)


def solution(mesh):
    in_specs = (P("lat", "lon", None), P(), P(), P(), P("lat", "lon", None))
    out_specs = (
        P("lat", "lon", None),
        P("lat", "lon", None),
        P(None, None, "lat"),
        P(None, None, "lat"),
        P(None, None, "lat"),
    )
    return jax.shard_map(
        on_device, mesh=mesh, in_specs=in_specs, out_specs=out_specs, check_vma=False
    )
```

```python
import jax
import jax.numpy as jnp
from jax import lax
from jax.sharding import PartitionSpec as P


def exchange(x, h):
    nlat, nlon = lax.axis_size("lat"), lax.axis_size("lon")
    left = lax.ppermute(x[:, -h:], "lon", [(j, (j + 1) % nlon) for j in range(nlon)])
    right = lax.ppermute(x[:, :h], "lon", [(j, (j - 1) % nlon) for j in range(nlon)])
    x = jnp.concatenate([left, x, right], axis=1)
    top = lax.ppermute(x[-h:], "lat", [(i, i + 1) for i in range(nlat - 1)])
    bottom = lax.ppermute(x[:h], "lat", [(i + 1, i) for i in range(nlat - 1)])
    return jnp.concatenate([top, x, bottom], axis=0)


def inside(x, own_rows, h):
    first = lax.axis_index("lat") * own_rows - h
    rows = first + lax.broadcasted_iota(jnp.int32, (x.shape[0], 1, 1), 0)
    keep = (rows >= 0) & (rows < own_rows * lax.axis_size("lat"))
    return jnp.where(keep, x, jnp.zeros_like(x))


def crop(x, h):
    return x[h : x.shape[0] - h, h : x.shape[1] - h]


def gelu(z):
    return 0.5 * z * (1.0 + jax.scipy.special.erf(z * 0.7071067811865476))


def gelu_slope(z):
    return (
        0.5 * (1.0 + jax.scipy.special.erf(z * 0.7071067811865476))
        + z * jnp.exp(-0.5 * z * z) * 0.3989422804014327
    )


def forward_conv(padded, kernel):
    out_rows, out_cols = (padded.shape[0] - 2, padded.shape[1] - 2)
    total = jnp.zeros((out_rows, out_cols, kernel.shape[2]), jnp.float32)
    for tap in range(9):
        shift_a, shift_b = divmod(tap, 3)
        piece = padded[shift_a : shift_a + out_rows, shift_b : shift_b + out_cols]
        total = total + jnp.einsum(
            "rci,io->rco", piece, kernel[tap], preferred_element_type=jnp.float32
        )
    return total


def adjoint_conv(padded, kernel):
    out_rows, out_cols = (padded.shape[0] - 2, padded.shape[1] - 2)
    total = jnp.zeros((out_rows, out_cols, kernel.shape[1]), jnp.float32)
    for tap in range(9):
        shift_a, shift_b = divmod(tap, 3)
        piece = padded[2 - shift_a : 2 - shift_a + out_rows, 2 - shift_b : 2 - shift_b + out_cols]
        total = total + jnp.einsum(
            "rco,io->rci", piece, kernel[tap], preferred_element_type=jnp.float32
        )
    return total


def gray(n_bits, low):
    def label(i):
        ring = (i >> low) & ((1 << n_bits) - 1)
        return (i & ~(((1 << n_bits) - 1) << low)) | ((ring ^ (ring >> 1)) << low)
    return label


def labels(axis):
    n = lax.axis_size(axis)
    label = gray(2, 2) if axis == "lat" else gray(3, 0)
    lab = [label(i) for i in range(n)]
    pos = [0] * n
    for i, l in enumerate(lab):
        pos[l] = i
    return lab, pos


def halve(x, axis, order=None):
    n = lax.axis_size(axis)
    bits = n.bit_length() - 1
    order = tuple(range(bits)) if order is None else tuple(b for b in order if b < bits)
    lab, pos = labels(axis)
    runs, first = [], 0
    for l in range(1, n + 1):
        if l == n or pos[l] != pos[l - 1] + 1:
            runs.append(x[pos[first] : pos[l - 1] + 1])
            first = l
    x = jnp.concatenate(runs) if len(runs) > 1 else x
    me = jnp.asarray(lab, jnp.int32)[lax.axis_index(axis)]
    x = x.reshape((2,) * bits + x.shape[1:])
    left = list(range(bits - 1, -1, -1))
    for b in order:
        dim = left.index(b)
        left.remove(b)
        mine = (me >> b) & 1
        keep = lax.dynamic_index_in_dim(x, mine, dim, keepdims=False)
        send = lax.dynamic_index_in_dim(x, 1 - mine, dim, keepdims=False)
        x = keep + lax.ppermute(send, axis, [(i, pos[lab[i] ^ (1 << b)]) for i in range(n)])
    return x


def all_sum(x, axis, order=None):
    n = lax.axis_size(axis)
    lab, pos = labels(axis)
    bits = n.bit_length() - 1
    order = tuple(range(bits)) if order is None else tuple(b for b in order if b < bits)
    for b in order:
        x = x + lax.ppermute(x, axis, [(i, pos[lab[i] ^ (1 << b)]) for i in range(n)])
    return x


def kernel_grad(padded, delta, lat_order, lon_order):
    own_rows, own_cols = (delta.shape[0], delta.shape[1])
    cells = own_rows * lax.axis_size("lat") * own_cols * lax.axis_size("lon")
    scale = 1.0 / float(cells) ** 0.5
    terms = []
    for tap in range(9):
        shift_a, shift_b = divmod(tap, 3)
        piece = padded[shift_a : shift_a + own_rows, shift_b : shift_b + own_cols]
        terms.append(
            jnp.einsum("rci,rco->oi", piece, delta, preferred_element_type=jnp.float32) * scale
        )
    local_term = jnp.stack(terms, axis=1)
    n_out, taps, n_in = local_term.shape
    nlat = lax.axis_size("lat")
    owned = halve(local_term.reshape(nlat, -1, 128), "lat", lat_order)
    owned = all_sum(owned, "lon", lon_order)
    return owned.reshape(n_out // nlat, taps, n_in).transpose(1, 2, 0)


def on_device(fields, kernel_first, kernel_second, kernel_third, cotangent):
    own_rows = fields.shape[0]
    width = fields.shape[2]
    both = exchange(jnp.concatenate([fields, cotangent], axis=2), 4)
    fields_4, cotangent_3 = both[..., :width], crop(both[..., width:], 1)
    pre_first = forward_conv(fields_4, kernel_first)
    act_first = inside(gelu(pre_first).astype(jnp.bfloat16), own_rows, 3)
    pre_second = forward_conv(act_first, kernel_second)
    act_second = inside(gelu(crop(pre_second, 1)).astype(jnp.bfloat16), own_rows, 1)
    output = forward_conv(act_second, kernel_third)
    grad_third = kernel_grad(act_second, crop(cotangent_3, 3), (0, 1, 2, 3), (0, 1, 2, 3))
    delta_second = inside(
        (adjoint_conv(cotangent_3, kernel_third) * gelu_slope(pre_second)).astype(jnp.bfloat16),
        own_rows, 2,
    )
    delta_first = inside(
        (adjoint_conv(delta_second, kernel_second) * gelu_slope(crop(pre_first, 2))).astype(
            jnp.bfloat16
        ),
        own_rows, 1,
    )
    grad_second = kernel_grad(crop(act_first, 2), crop(delta_second, 2), (0, 2, 1, 3), (1, 2, 3, 0))
    field_grad = adjoint_conv(delta_first, kernel_first)
    grad_first = kernel_grad(crop(fields_4, 3), crop(delta_first, 1), (0, 3, 2, 1), (2, 3, 0, 1))
    return (output, field_grad, grad_first, grad_second, grad_third)


def solution(mesh):
    in_specs = (P("lat", "lon", None), P(), P(), P(), P("lat", "lon", None))
    out_specs = (
        P("lat", "lon", None),
        P("lat", "lon", None),
        P(None, None, "lat"),
        P(None, None, "lat"),
        P(None, None, "lat"),
    )
    return jax.shard_map(
        on_device, mesh=mesh, in_specs=in_specs, out_specs=out_specs, check_vma=False
    )
```

```python
import jax
import jax.numpy as jnp
from jax import lax
from jax.sharding import PartitionSpec as P


def exchange(x, h):
    nlat, nlon = lax.axis_size("lat"), lax.axis_size("lon")
    left = lax.ppermute(x[:, -h:], "lon", [(j, (j + 1) % nlon) for j in range(nlon)])
    right = lax.ppermute(x[:, :h], "lon", [(j, (j - 1) % nlon) for j in range(nlon)])
    x = jnp.concatenate([left, x, right], axis=1)
    top = lax.ppermute(x[-h:], "lat", [(i, i + 1) for i in range(nlat - 1)])
    bottom = lax.ppermute(x[:h], "lat", [(i + 1, i) for i in range(nlat - 1)])
    return jnp.concatenate([top, x, bottom], axis=0)


def inside(x, own_rows, h):
    first = lax.axis_index("lat") * own_rows - h
    rows = first + lax.broadcasted_iota(jnp.int32, (x.shape[0], 1, 1), 0)
    keep = (rows >= 0) & (rows < own_rows * lax.axis_size("lat"))
    return jnp.where(keep, x, jnp.zeros_like(x))


def crop(x, h):
    return x[h : x.shape[0] - h, h : x.shape[1] - h]


def gelu(z):
    return 0.5 * z * (1.0 + jax.scipy.special.erf(z * 0.7071067811865476))


def gelu_slope(z):
    return (
        0.5 * (1.0 + jax.scipy.special.erf(z * 0.7071067811865476))
        + z * jnp.exp(-0.5 * z * z) * 0.3989422804014327
    )


def forward_conv(padded, kernel):
    out_rows, out_cols = (padded.shape[0] - 2, padded.shape[1] - 2)
    total = jnp.zeros((out_rows, out_cols, kernel.shape[2]), jnp.float32)
    for tap in range(9):
        shift_a, shift_b = divmod(tap, 3)
        piece = padded[shift_a : shift_a + out_rows, shift_b : shift_b + out_cols]
        total = total + jnp.einsum(
            "rci,io->rco", piece, kernel[tap], preferred_element_type=jnp.float32
        )
    return total


def adjoint_conv(padded, kernel):
    out_rows, out_cols = (padded.shape[0] - 2, padded.shape[1] - 2)
    total = jnp.zeros((out_rows, out_cols, kernel.shape[1]), jnp.float32)
    for tap in range(9):
        shift_a, shift_b = divmod(tap, 3)
        piece = padded[2 - shift_a : 2 - shift_a + out_rows, 2 - shift_b : 2 - shift_b + out_cols]
        total = total + jnp.einsum(
            "rco,io->rci", piece, kernel[tap], preferred_element_type=jnp.float32
        )
    return total


def gray(n_bits, low):
    def label(i):
        ring = (i >> low) & ((1 << n_bits) - 1)
        return (i & ~(((1 << n_bits) - 1) << low)) | ((ring ^ (ring >> 1)) << low)
    return label


def labels(axis):
    n = lax.axis_size(axis)
    label = gray(2, 2) if axis == "lat" else gray(3, 0)
    lab = [label(i) for i in range(n)]
    pos = [0] * n
    for i, l in enumerate(lab):
        pos[l] = i
    return lab, pos


def in_label_order(x, axis):
    n = lax.axis_size(axis)
    block = x.shape[0] // n
    lab, pos = labels(axis)
    runs, first = [], 0
    for l in range(1, n + 1):
        if l == n or pos[l] != pos[l - 1] + 1:
            runs.append(x[pos[first] * block : (pos[l - 1] + 1) * block])
            first = l
    return jnp.concatenate(runs) if len(runs) > 1 else x


def halve(x, axis, order=None):
    n = lax.axis_size(axis)
    bits = n.bit_length() - 1
    order = tuple(range(bits)) if order is None else tuple(b for b in order if b < bits)
    lab, pos = labels(axis)
    me = jnp.asarray(lab, jnp.int32)[lax.axis_index(axis)]
    x = x.reshape((2,) * bits + x.shape[1:])
    left = list(range(bits - 1, -1, -1))
    for b in order:
        dim = left.index(b)
        left.remove(b)
        mine = (me >> b) & 1
        keep = lax.dynamic_index_in_dim(x, mine, dim, keepdims=False)
        send = lax.dynamic_index_in_dim(x, 1 - mine, dim, keepdims=False)
        x = keep + lax.ppermute(send, axis, [(i, pos[lab[i] ^ (1 << b)]) for i in range(n)])
    return x


def all_sum(x, axis, order=None):
    n = lax.axis_size(axis)
    lab, pos = labels(axis)
    bits = n.bit_length() - 1
    order = tuple(range(bits)) if order is None else tuple(b for b in order if b < bits)
    for b in order:
        x = x + lax.ppermute(x, axis, [(i, pos[lab[i] ^ (1 << b)]) for i in range(n)])
    return x


def kernel_grad(padded, delta, lat_order, lon_order):
    own_rows, own_cols = (delta.shape[0], delta.shape[1])
    cells = own_rows * lax.axis_size("lat") * own_cols * lax.axis_size("lon")
    scale = 1.0 / float(cells) ** 0.5
    terms = []
    for tap in range(9):
        shift_a, shift_b = divmod(tap, 3)
        piece = padded[shift_a : shift_a + own_rows, shift_b : shift_b + own_cols]
        terms.append(
            in_label_order(
                jnp.einsum("rci,rco->oi", piece, delta, preferred_element_type=jnp.float32) * scale,
                "lat",
            )
        )
    local_term = jnp.stack(terms, axis=1)
    n_out, taps, n_in = local_term.shape
    nlat = lax.axis_size("lat")
    owned = halve(local_term.reshape(nlat, -1, 128), "lat", lat_order)
    owned = all_sum(owned, "lon", lon_order)
    return owned.reshape(n_out // nlat, taps, n_in).transpose(1, 2, 0)


def on_device(fields, kernel_first, kernel_second, kernel_third, cotangent):
    own_rows = fields.shape[0]
    width = fields.shape[2]
    both = exchange(jnp.concatenate([fields, cotangent], axis=2), 4)
    fields_4, cotangent_3 = both[..., :width], crop(both[..., width:], 1)
    pre_first = forward_conv(fields_4, kernel_first)
    act_first = inside(gelu(pre_first).astype(jnp.bfloat16), own_rows, 3)
    pre_second = forward_conv(act_first, kernel_second)
    act_second = inside(gelu(crop(pre_second, 1)).astype(jnp.bfloat16), own_rows, 1)
    output = forward_conv(act_second, kernel_third)
    grad_third = kernel_grad(act_second, crop(cotangent_3, 3), (0, 1, 2, 3), (0, 1, 2, 3))
    delta_second = inside(
        (adjoint_conv(cotangent_3, kernel_third) * gelu_slope(pre_second)).astype(jnp.bfloat16),
        own_rows, 2,
    )
    delta_first = inside(
        (adjoint_conv(delta_second, kernel_second) * gelu_slope(crop(pre_first, 2))).astype(
            jnp.bfloat16
        ),
        own_rows, 1,
    )
    grad_second = kernel_grad(crop(act_first, 2), crop(delta_second, 2), (0, 2, 1, 3), (1, 2, 3, 0))
    field_grad = adjoint_conv(delta_first, kernel_first)
    grad_first = kernel_grad(crop(fields_4, 3), crop(delta_first, 1), (0, 3, 2, 1), (2, 3, 0, 1))
    return (output, field_grad, grad_first, grad_second, grad_third)


def solution(mesh):
    in_specs = (P("lat", "lon", None), P(), P(), P(), P("lat", "lon", None))
    out_specs = (
        P("lat", "lon", None),
        P("lat", "lon", None),
        P(None, None, "lat"),
        P(None, None, "lat"),
        P(None, None, "lat"),
    )
    return jax.shard_map(
        on_device, mesh=mesh, in_specs=in_specs, out_specs=out_specs, check_vma=False
    )
```

```python
import jax
import jax.numpy as jnp
from jax import lax
from jax.sharding import PartitionSpec as P


def exchange(x, h):
    nlat, nlon = lax.axis_size("lat"), lax.axis_size("lon")
    left = lax.ppermute(x[:, -h:], "lon", [(j, (j + 1) % nlon) for j in range(nlon)])
    right = lax.ppermute(x[:, :h], "lon", [(j, (j - 1) % nlon) for j in range(nlon)])
    x = jnp.concatenate([left, x, right], axis=1)
    top = lax.ppermute(x[-h:], "lat", [(i, i + 1) for i in range(nlat - 1)])
    bottom = lax.ppermute(x[:h], "lat", [(i + 1, i) for i in range(nlat - 1)])
    return jnp.concatenate([top, x, bottom], axis=0)


def inside(x, own_rows, h):
    first = lax.axis_index("lat") * own_rows - h
    rows = first + lax.broadcasted_iota(jnp.int32, (x.shape[0], 1, 1), 0)
    keep = (rows >= 0) & (rows < own_rows * lax.axis_size("lat"))
    return jnp.where(keep, x, jnp.zeros_like(x))


def crop(x, h):
    return x[h : x.shape[0] - h, h : x.shape[1] - h]


def gelu(z):
    return 0.5 * z * (1.0 + jax.scipy.special.erf(z * 0.7071067811865476))


def gelu_slope(z):
    return (
        0.5 * (1.0 + jax.scipy.special.erf(z * 0.7071067811865476))
        + z * jnp.exp(-0.5 * z * z) * 0.3989422804014327
    )


def forward_conv(padded, kernel):
    out_rows, out_cols = (padded.shape[0] - 2, padded.shape[1] - 2)
    total = jnp.zeros((out_rows, out_cols, kernel.shape[2]), jnp.float32)
    for tap in range(9):
        shift_a, shift_b = divmod(tap, 3)
        piece = padded[shift_a : shift_a + out_rows, shift_b : shift_b + out_cols]
        total = total + jnp.einsum(
            "rci,io->rco", piece, kernel[tap], preferred_element_type=jnp.float32
        )
    return total


def adjoint_conv(padded, kernel):
    out_rows, out_cols = (padded.shape[0] - 2, padded.shape[1] - 2)
    total = jnp.zeros((out_rows, out_cols, kernel.shape[1]), jnp.float32)
    for tap in range(9):
        shift_a, shift_b = divmod(tap, 3)
        piece = padded[2 - shift_a : 2 - shift_a + out_rows, 2 - shift_b : 2 - shift_b + out_cols]
        total = total + jnp.einsum(
            "rco,io->rci", piece, kernel[tap], preferred_element_type=jnp.float32
        )
    return total


def gray(n_bits, low):
    def label(i):
        ring = (i >> low) & ((1 << n_bits) - 1)
        return (i & ~(((1 << n_bits) - 1) << low)) | ((ring ^ (ring >> 1)) << low)
    return label


def labels(axis):
    n = lax.axis_size(axis)
    label = (lambda i: i) if axis == "lat" else gray(3, 0)
    lab = [label(i) for i in range(n)]
    pos = [0] * n
    for i, l in enumerate(lab):
        pos[l] = i
    return lab, pos


def halve(x, axis, order=None):
    n = lax.axis_size(axis)
    bits = n.bit_length() - 1
    order = tuple(range(bits)) if order is None else tuple(b for b in order if b < bits)
    lab, pos = labels(axis)
    runs, first = [], 0
    for l in range(1, n + 1):
        if l == n or pos[l] != pos[l - 1] + 1:
            runs.append(x[pos[first] : pos[l - 1] + 1])
            first = l
    x = jnp.concatenate(runs) if len(runs) > 1 else x
    me = jnp.asarray(lab, jnp.int32)[lax.axis_index(axis)]
    x = x.reshape((2,) * bits + x.shape[1:])
    left = list(range(bits - 1, -1, -1))
    for b in order:
        dim = left.index(b)
        left.remove(b)
        mine = (me >> b) & 1
        keep = lax.dynamic_index_in_dim(x, mine, dim, keepdims=False)
        send = lax.dynamic_index_in_dim(x, 1 - mine, dim, keepdims=False)
        x = keep + lax.ppermute(send, axis, [(i, pos[lab[i] ^ (1 << b)]) for i in range(n)])
    return x


def all_sum(x, axis, order=None):
    n = lax.axis_size(axis)
    lab, pos = labels(axis)
    bits = n.bit_length() - 1
    order = tuple(range(bits)) if order is None else tuple(b for b in order if b < bits)
    for b in order:
        x = x + lax.ppermute(x, axis, [(i, pos[lab[i] ^ (1 << b)]) for i in range(n)])
    return x


def kernel_grad(padded, delta, lat_order, lon_order):
    own_rows, own_cols = (delta.shape[0], delta.shape[1])
    cells = own_rows * lax.axis_size("lat") * own_cols * lax.axis_size("lon")
    scale = 1.0 / float(cells) ** 0.5
    terms = []
    for tap in range(9):
        shift_a, shift_b = divmod(tap, 3)
        piece = padded[shift_a : shift_a + own_rows, shift_b : shift_b + own_cols]
        terms.append(
            jnp.einsum("rci,rco->oi", piece, delta, preferred_element_type=jnp.float32) * scale
        )
    local_term = jnp.stack(terms, axis=1)
    n_out, taps, n_in = local_term.shape
    nlat = lax.axis_size("lat")
    owned = halve(local_term.reshape(nlat, -1, 128), "lat", lat_order)
    owned = all_sum(owned, "lon", lon_order)
    return owned.reshape(n_out // nlat, taps, n_in).transpose(1, 2, 0)


def on_device(fields, kernel_first, kernel_second, kernel_third, cotangent):
    own_rows = fields.shape[0]
    width = fields.shape[2]
    both = exchange(jnp.concatenate([fields, cotangent], axis=2), 4)
    fields_4, cotangent_3 = both[..., :width], crop(both[..., width:], 1)
    pre_first = forward_conv(fields_4, kernel_first)
    act_first = inside(gelu(pre_first).astype(jnp.bfloat16), own_rows, 3)
    pre_second = forward_conv(act_first, kernel_second)
    act_second = inside(gelu(crop(pre_second, 1)).astype(jnp.bfloat16), own_rows, 1)
    output = forward_conv(act_second, kernel_third)
    grad_third = kernel_grad(act_second, crop(cotangent_3, 3), (0, 1, 2, 3), (0, 1, 2, 3))
    delta_second = inside(
        (adjoint_conv(cotangent_3, kernel_third) * gelu_slope(pre_second)).astype(jnp.bfloat16),
        own_rows, 2,
    )
    delta_first = inside(
        (adjoint_conv(delta_second, kernel_second) * gelu_slope(crop(pre_first, 2))).astype(
            jnp.bfloat16
        ),
        own_rows, 1,
    )
    grad_second = kernel_grad(crop(act_first, 2), crop(delta_second, 2), (0, 2, 1, 3), (1, 2, 3, 0))
    field_grad = adjoint_conv(delta_first, kernel_first)
    grad_first = kernel_grad(crop(fields_4, 3), crop(delta_first, 1), (0, 3, 2, 1), (2, 3, 0, 1))
    return (output, field_grad, grad_first, grad_second, grad_third)


def solution(mesh):
    in_specs = (P("lat", "lon", None), P(), P(), P(), P("lat", "lon", None))
    out_specs = (
        P("lat", "lon", None),
        P("lat", "lon", None),
        P(None, None, "lat"),
        P(None, None, "lat"),
        P(None, None, "lat"),
    )
    return jax.shard_map(
        on_device, mesh=mesh, in_specs=in_specs, out_specs=out_specs, check_vma=False
    )
```

```python
import jax
import jax.numpy as jnp
from jax import lax
from jax.sharding import PartitionSpec as P


def exchange(x, h):
    nlat, nlon = lax.axis_size("lat"), lax.axis_size("lon")
    left = lax.ppermute(x[:, -h:], "lon", [(j, (j + 1) % nlon) for j in range(nlon)])
    right = lax.ppermute(x[:, :h], "lon", [(j, (j - 1) % nlon) for j in range(nlon)])
    x = jnp.concatenate([left, x, right], axis=1)
    top = lax.ppermute(x[-h:], "lat", [(i, i + 1) for i in range(nlat - 1)])
    bottom = lax.ppermute(x[:h], "lat", [(i + 1, i) for i in range(nlat - 1)])
    return jnp.concatenate([top, x, bottom], axis=0)


def inside(x, own_rows, h):
    first = lax.axis_index("lat") * own_rows - h
    rows = first + lax.broadcasted_iota(jnp.int32, (x.shape[0], 1, 1), 0)
    keep = (rows >= 0) & (rows < own_rows * lax.axis_size("lat"))
    return jnp.where(keep, x, jnp.zeros_like(x))


def crop(x, h):
    return x[h : x.shape[0] - h, h : x.shape[1] - h]


def gelu(z):
    return 0.5 * z * (1.0 + jax.scipy.special.erf(z * 0.7071067811865476))


def gelu_slope(z):
    return (
        0.5 * (1.0 + jax.scipy.special.erf(z * 0.7071067811865476))
        + z * jnp.exp(-0.5 * z * z) * 0.3989422804014327
    )


def forward_conv(padded, kernel):
    out_rows, out_cols = (padded.shape[0] - 2, padded.shape[1] - 2)
    total = jnp.zeros((out_rows, out_cols, kernel.shape[2]), jnp.float32)
    for tap in range(9):
        shift_a, shift_b = divmod(tap, 3)
        piece = padded[shift_a : shift_a + out_rows, shift_b : shift_b + out_cols]
        total = total + jnp.einsum(
            "rci,io->rco", piece, kernel[tap], preferred_element_type=jnp.float32
        )
    return total


def adjoint_conv(padded, kernel):
    out_rows, out_cols = (padded.shape[0] - 2, padded.shape[1] - 2)
    total = jnp.zeros((out_rows, out_cols, kernel.shape[1]), jnp.float32)
    for tap in range(9):
        shift_a, shift_b = divmod(tap, 3)
        piece = padded[2 - shift_a : 2 - shift_a + out_rows, 2 - shift_b : 2 - shift_b + out_cols]
        total = total + jnp.einsum(
            "rco,io->rci", piece, kernel[tap], preferred_element_type=jnp.float32
        )
    return total


def gray(n_bits, low):
    def label(i):
        ring = (i >> low) & ((1 << n_bits) - 1)
        return (i & ~(((1 << n_bits) - 1) << low)) | ((ring ^ (ring >> 1)) << low)
    return label


def labels(axis):
    n = lax.axis_size(axis)
    label = gray(2, 2) if axis == "lat" else gray(3, 0)
    lab = [label(i) for i in range(n)]
    pos = [0] * n
    for i, l in enumerate(lab):
        pos[l] = i
    return lab, pos


def halve(x, axis, order=None):
    n = lax.axis_size(axis)
    bits = n.bit_length() - 1
    order = tuple(range(bits)) if order is None else tuple(b for b in order if b < bits)
    lab, pos = labels(axis)
    runs, first = [], 0
    for l in range(1, n + 1):
        if l == n or pos[l] != pos[l - 1] + 1:
            runs.append(x[pos[first] : pos[l - 1] + 1])
            first = l
    x = jnp.concatenate(runs) if len(runs) > 1 else x
    me = jnp.asarray(lab, jnp.int32)[lax.axis_index(axis)]
    x = x.reshape((2,) * bits + x.shape[1:])
    left = list(range(bits - 1, -1, -1))
    for b in order:
        dim = left.index(b)
        left.remove(b)
        mine = (me >> b) & 1
        keep = lax.dynamic_index_in_dim(x, mine, dim, keepdims=False)
        send = lax.dynamic_index_in_dim(x, 1 - mine, dim, keepdims=False)
        x = keep + lax.ppermute(send, axis, [(i, pos[lab[i] ^ (1 << b)]) for i in range(n)])
    return x


def all_sum(x, axis, order=None):
    n = lax.axis_size(axis)
    lab, pos = labels(axis)
    bits = n.bit_length() - 1
    order = tuple(range(bits)) if order is None else tuple(b for b in order if b < bits)
    for b in order:
        x = x + lax.ppermute(x, axis, [(i, pos[lab[i] ^ (1 << b)]) for i in range(n)])
    return x


def kernel_grad(padded, delta, lat_order, lon_order):
    own_rows, own_cols = (delta.shape[0], delta.shape[1])
    cells = own_rows * lax.axis_size("lat") * own_cols * lax.axis_size("lon")
    scale = 1.0 / float(cells) ** 0.5
    terms = []
    for tap in range(9):
        shift_a, shift_b = divmod(tap, 3)
        piece = padded[shift_a : shift_a + own_rows, shift_b : shift_b + own_cols]
        terms.append(
            jnp.einsum("rci,rco->oi", piece, delta, preferred_element_type=jnp.float32) * scale
        )
    local_term = jnp.stack(terms, axis=1)
    n_out, taps, n_in = local_term.shape
    nlat = lax.axis_size("lat")
    owned = halve(local_term.reshape(nlat, -1, 128), "lat", lat_order)
    owned = all_sum(owned, "lon", lon_order)
    return owned.reshape(n_out // nlat, taps, n_in).transpose(1, 2, 0)


def on_device(fields, kernel_first, kernel_second, kernel_third, cotangent):
    own_rows = fields.shape[0]
    width = fields.shape[2]
    both = exchange(jnp.concatenate([fields, cotangent], axis=2), 4)
    fields_4, cotangent_3 = both[..., :width], crop(both[..., width:], 1)
    pre_first = forward_conv(fields_4, kernel_first)
    act_first = inside(gelu(pre_first).astype(jnp.bfloat16), own_rows, 3)
    pre_second = forward_conv(act_first, kernel_second)
    act_second = inside(gelu(crop(pre_second, 1)).astype(jnp.bfloat16), own_rows, 1)
    output = forward_conv(act_second, kernel_third)
    grad_third = kernel_grad(act_second, crop(cotangent_3, 3), (0, 1, 2, 3), (0, 1, 2, 3))
    delta_second = inside(
        (adjoint_conv(cotangent_3, kernel_third) * gelu_slope(pre_second)).astype(jnp.bfloat16),
        own_rows, 2,
    )
    delta_first = inside(
        (adjoint_conv(delta_second, kernel_second) * gelu_slope(crop(pre_first, 2))).astype(
            jnp.bfloat16
        ),
        own_rows, 1,
    )
    grad_second = kernel_grad(crop(act_first, 2), crop(delta_second, 2), (0, 2, 3, 1), (1, 2, 3, 0))
    field_grad = adjoint_conv(delta_first, kernel_first)
    grad_first = kernel_grad(crop(fields_4, 3), crop(delta_first, 1), (0, 3, 2, 1), (2, 3, 0, 1))
    return (output, field_grad, grad_first, grad_second, grad_third)


def solution(mesh):
    in_specs = (P("lat", "lon", None), P(), P(), P(), P("lat", "lon", None))
    out_specs = (
        P("lat", "lon", None),
        P("lat", "lon", None),
        P(None, None, "lat"),
        P(None, None, "lat"),
        P(None, None, "lat"),
    )
    return jax.shard_map(
        on_device, mesh=mesh, in_specs=in_specs, out_specs=out_specs, check_vma=False
    )
```

```python
import jax
import jax.numpy as jnp
from jax import lax
from jax.sharding import PartitionSpec as P


def exchange(x, h):
    nlat, nlon = lax.axis_size("lat"), lax.axis_size("lon")
    left = lax.ppermute(x[:, -h:], "lon", [(j, (j + 1) % nlon) for j in range(nlon)])
    right = lax.ppermute(x[:, :h], "lon", [(j, (j - 1) % nlon) for j in range(nlon)])
    x = jnp.concatenate([left, x, right], axis=1)
    top = lax.ppermute(x[-h:], "lat", [(i, i + 1) for i in range(nlat - 1)])
    bottom = lax.ppermute(x[:h], "lat", [(i + 1, i) for i in range(nlat - 1)])
    return jnp.concatenate([top, x, bottom], axis=0)


def inside(x, own_rows, h):
    first = lax.axis_index("lat") * own_rows - h
    rows = first + lax.broadcasted_iota(jnp.int32, (x.shape[0], 1, 1), 0)
    keep = (rows >= 0) & (rows < own_rows * lax.axis_size("lat"))
    return jnp.where(keep, x, jnp.zeros_like(x))


def crop(x, h):
    return x[h : x.shape[0] - h, h : x.shape[1] - h]


def gelu(z):
    return 0.5 * z * (1.0 + jax.scipy.special.erf(z * 0.7071067811865476))


def gelu_slope(z):
    return (
        0.5 * (1.0 + jax.scipy.special.erf(z * 0.7071067811865476))
        + z * jnp.exp(-0.5 * z * z) * 0.3989422804014327
    )


def forward_conv(padded, kernel):
    out_rows, out_cols = (padded.shape[0] - 2, padded.shape[1] - 2)
    total = jnp.zeros((out_rows, out_cols, kernel.shape[2]), jnp.float32)
    for tap in range(9):
        shift_a, shift_b = divmod(tap, 3)
        piece = padded[shift_a : shift_a + out_rows, shift_b : shift_b + out_cols]
        total = total + jnp.einsum(
            "rci,io->rco", piece, kernel[tap], preferred_element_type=jnp.float32
        )
    return total


def adjoint_conv(padded, kernel):
    out_rows, out_cols = (padded.shape[0] - 2, padded.shape[1] - 2)
    total = jnp.zeros((out_rows, out_cols, kernel.shape[1]), jnp.float32)
    for tap in range(9):
        shift_a, shift_b = divmod(tap, 3)
        piece = padded[2 - shift_a : 2 - shift_a + out_rows, 2 - shift_b : 2 - shift_b + out_cols]
        total = total + jnp.einsum(
            "rco,io->rci", piece, kernel[tap], preferred_element_type=jnp.float32
        )
    return total


def gray(n_bits, low):
    def label(i):
        ring = (i >> low) & ((1 << n_bits) - 1)
        return (i & ~(((1 << n_bits) - 1) << low)) | ((ring ^ (ring >> 1)) << low)
    return label


def labels(axis):
    n = lax.axis_size(axis)
    label = gray(2, 2) if axis == "lat" else gray(3, 0)
    lab = [label(i) for i in range(n)]
    pos = [0] * n
    for i, l in enumerate(lab):
        pos[l] = i
    return lab, pos


def halve(x, axis, order=None):
    n = lax.axis_size(axis)
    bits = n.bit_length() - 1
    order = tuple(range(bits)) if order is None else tuple(b for b in order if b < bits)
    lab, pos = labels(axis)
    runs, first = [], 0
    for l in range(1, n + 1):
        if l == n or pos[l] != pos[l - 1] + 1:
            runs.append(x[pos[first] : pos[l - 1] + 1])
            first = l
    x = jnp.concatenate(runs) if len(runs) > 1 else x
    me = jnp.asarray(lab, jnp.int32)[lax.axis_index(axis)]
    x = x.reshape((2,) * bits + x.shape[1:])
    left = list(range(bits - 1, -1, -1))
    for b in order:
        dim = left.index(b)
        left.remove(b)
        mine = (me >> b) & 1
        keep = lax.dynamic_index_in_dim(x, mine, dim, keepdims=False)
        send = lax.dynamic_index_in_dim(x, 1 - mine, dim, keepdims=False)
        x = keep + lax.ppermute(send, axis, [(i, pos[lab[i] ^ (1 << b)]) for i in range(n)])
    return x


def all_sum(x, axis, order=None):
    n = lax.axis_size(axis)
    lab, pos = labels(axis)
    bits = n.bit_length() - 1
    order = tuple(range(bits)) if order is None else tuple(b for b in order if b < bits)
    for b in order:
        x = x + lax.ppermute(x, axis, [(i, pos[lab[i] ^ (1 << b)]) for i in range(n)])
    return x


def kernel_grad(padded, delta, lat_order, lon_order):
    own_rows, own_cols = (delta.shape[0], delta.shape[1])
    cells = own_rows * lax.axis_size("lat") * own_cols * lax.axis_size("lon")
    scale = 1.0 / float(cells) ** 0.5
    terms = []
    for tap in range(9):
        shift_a, shift_b = divmod(tap, 3)
        piece = padded[shift_a : shift_a + own_rows, shift_b : shift_b + own_cols]
        terms.append(
            jnp.einsum("rci,rco->oi", piece, delta, preferred_element_type=jnp.float32) * scale
        )
    local_term = jnp.stack(terms, axis=1)
    n_out, taps, n_in = local_term.shape
    nlat = lax.axis_size("lat")
    owned = halve(local_term.reshape(nlat, -1, 128), "lat", lat_order)
    owned = all_sum(owned, "lon", lon_order)
    return owned.reshape(n_out // nlat, taps, n_in).transpose(1, 2, 0)


def on_device(fields, kernel_first, kernel_second, kernel_third, cotangent):
    own_rows = fields.shape[0]
    width = fields.shape[2]
    both = exchange(jnp.concatenate([fields, cotangent], axis=2), 4)
    fields_4, cotangent_3 = both[..., :width], crop(both[..., width:], 1)
    pre_first = forward_conv(fields_4, kernel_first)
    act_first = inside(gelu(pre_first).astype(jnp.bfloat16), own_rows, 3)
    pre_second = forward_conv(act_first, kernel_second)
    act_second = inside(gelu(crop(pre_second, 1)).astype(jnp.bfloat16), own_rows, 1)
    output = forward_conv(act_second, kernel_third)
    grad_third = kernel_grad(act_second, crop(cotangent_3, 3), (0, 3, 1, 2), (0, 1, 2, 3))
    delta_second = inside(
        (adjoint_conv(cotangent_3, kernel_third) * gelu_slope(pre_second)).astype(jnp.bfloat16),
        own_rows, 2,
    )
    delta_first = inside(
        (adjoint_conv(delta_second, kernel_second) * gelu_slope(crop(pre_first, 2))).astype(
            jnp.bfloat16
        ),
        own_rows, 1,
    )
    grad_second = kernel_grad(crop(act_first, 2), crop(delta_second, 2), (0, 2, 1, 3), (1, 2, 3, 0))
    field_grad = adjoint_conv(delta_first, kernel_first)
    grad_first = kernel_grad(crop(fields_4, 3), crop(delta_first, 1), (0, 3, 2, 1), (2, 3, 0, 1))
    return (output, field_grad, grad_first, grad_second, grad_third)


def solution(mesh):
    in_specs = (P("lat", "lon", None), P(), P(), P(), P("lat", "lon", None))
    out_specs = (
        P("lat", "lon", None),
        P("lat", "lon", None),
        P(None, None, "lat"),
        P(None, None, "lat"),
        P(None, None, "lat"),
    )
    return jax.shard_map(
        on_device, mesh=mesh, in_specs=in_specs, out_specs=out_specs, check_vma=False
    )
```
